32 devices in a mesh: groups: 2 (over y), events: 8 (over z, x), heads: 2 (over core).
Axes of the slice: x: 2, y: 2, z: 4, core: 2. Of those that a mesh axis runs over, the one named last changes fastest.
Arguments:
- inputs: bfloat16 [256, 1024], P(('groups', 'events')), parts along dimension 0, may hold values from -6 to 6
- cand_user: int32 [256], P('groups'), parts along dimension 0, may hold values from 0 to 3, as said below
- event_user: int32 [8192], P(('groups', 'events')), parts along dimension 0, may hold values from 0 to 3, as said below
- event_count: int32 [16], P(('groups', 'events')), parts along dimension 0, may hold values from 128 to 512, as said below
- w_qu: bfloat16 [1024, 2, 1024], P(None, None, 'heads'), may hold values from -0.1875 to 0.1875
- keys: bfloat16 [8192, 1024], P(('groups', 'events'), 'heads'), parts along dimension 0, may hold values from -6 to 6
- values: bfloat16 [8192, 1024], P(('groups', 'events'), 'heads'), parts along dimension 0, may hold values from -6 to 6
- gain: float32 [1024], P('heads'), may hold values from 0.1 to 1.9
- w_out: bfloat16 [1024, 1024], P('heads'), may hold values from -0.1875 to 0.1875
Outputs:
- scored: bfloat16 [256, 1024], P(('groups', 'events')), parts along dimension 0
The draws below stay inside these ranges and needn't reach their ends.
There are 2 independent parts, one for each index of `groups`. The reference program is written for one: setup_inputs(seed, part) draws one part's arguments, and reference() takes and returns one part's arrays. A program takes and returns all parts, laid end to end along the dimension named above; an argument that names none is the same for every part. Nothing has to cross between parts.
Inputs may be any that keep to these rules, and one draw needn't show every extreme that they name: `event_count`: each cache shard's filled slots come first; some shard is full and some holds 128. `event_user`: Users' events are consecutive and in increasing user order over the whole cache; every user has 1 to 2047 events, and some user has exactly 2047. `cand_user`: every candidate belongs to a user that has at least one filled slot somewhere in the cache.
All inputs are finite; a program needn't handle non-finite values.
Results may differ from the reference program's by a relative error of at most 0.0075.
Values may be sent and summed in bfloat16 or wider, within the bound.
No kernel may reach another device: no remote copies, remote signals or barrier semaphores. Data moves between devices by JAX's collectives and lax.ppermute only.
A program may use at most 64 MiB of HBM per device.

```python
import math
import jax
import jax.numpy as jnp
from jax import lax

D = 1024
HEADS = 8
DH = 128
SPAN = 4
EV_DEV = 512
HD = 1024
SHARDS = 8
USERS = 4
CANDS = 128
EVENTS = 4096


def cache_layout(key):
    pair_key = jax.random.fold_in(key, 21)
    order_key = jax.random.fold_in(key, 22)
    count_key = jax.random.fold_in(key, 11)
    chosen_key = jax.random.fold_in(key, 12)
    slot_key = jax.random.fold_in(key, 23)
    shard_key = jax.random.fold_in(key, 24)
    pair_total = SPAN * EV_DEV
    halves = jax.random.randint(pair_key, (USERS // 2,), 1, pair_total)
    halves = halves.at[0].set(1)
    lengths = jnp.concatenate([halves, pair_total - halves]).astype(jnp.int32)
    order = jax.random.permutation(order_key, USERS)
    lengths = lengths[order]
    ends = jnp.cumsum(lengths).astype(jnp.int32)
    positions = jnp.arange(EVENTS, dtype=jnp.int32)
    event_user = jnp.sum((positions[:, None] >= ends[None, :]).astype(jnp.int32), axis=1).astype(jnp.int32)
    counts = jax.random.randint(count_key, (SHARDS,), EV_DEV // 4, EV_DEV + 1)
    chosen = jax.random.randint(chosen_key, (), 0, SHARDS)
    counts = counts.at[chosen].set(EV_DEV)
    counts = counts.at[(chosen + 1) % SHARDS].set(EV_DEV // 4)
    counts = counts.astype(jnp.int32)
    shard_pick = jax.random.randint(shard_key, (CANDS,), 0, SHARDS).astype(jnp.int32)
    raw_slots = jax.random.randint(slot_key, (CANDS,), 0, 1048576)
    slots = (raw_slots % counts[shard_pick]).astype(jnp.int32)
    cand_user = event_user[shard_pick * EV_DEV + slots]
    return (cand_user.astype(jnp.int32), event_user, counts)


def draw_cand_user(key, part):
    return cache_layout(key)[0]


def draw_event_user(key, part):
    return cache_layout(key)[1]


def draw_event_count(key, part):
    return cache_layout(key)[2]


def shard_levels(own_key, dims, split, low, largest):
    level = 1.0
    for position, blocks in split:
        heights = jax.random.uniform(jax.random.fold_in(jax.random.fold_in(own_key, 6), position), (blocks,), jnp.float32, low / len(split), largest / len(split))
        level = level * jnp.repeat(jnp.exp(heights), dims[position] // blocks).reshape((-1,) + (1,) * (len(dims) - 1 - position))
    return level


def bell_draw(stream_key, extent, deviation, reach, cuts=(), held_as=jnp.bfloat16):
    factor_of = shard_levels(stream_key, extent, cuts, -0.22, 0.18) if cuts else 1.0
    result = jax.random.normal(stream_key, extent, jnp.float32) * deviation * factor_of
    return jnp.minimum(jnp.maximum(result, -reach), reach).astype(held_as)


def setup_inputs(seed: int = 0, part: int = 0) -> dict:
    streams_of = jax.random.split(jax.random.key(seed), 10)
    own_keys = jax.random.split(jax.random.fold_in(streams_of[9], part), 10)
    return {
        "inputs": bell_draw(own_keys[0], (CANDS, D), 1.0, 6.0, ((0, 8),)),
        "cand_user": draw_cand_user(jax.random.fold_in(jax.random.fold_in(streams_of[9], part), 71), part),
        "event_user": draw_event_user(jax.random.fold_in(jax.random.fold_in(streams_of[9], part), 71), part),
        "event_count": draw_event_count(jax.random.fold_in(jax.random.fold_in(streams_of[9], part), 71), part),
        "w_qu": bell_draw(streams_of[4], (D, 2, HD), D ** -0.5, 0.1875, ((2, 2),)),
        "keys": bell_draw(own_keys[5], (EVENTS, HD), 1.0, 6.0, ((0, 8), (1, 2))),
        "values": bell_draw(own_keys[6], (EVENTS, HD), 1.0, 6.0, ((0, 8), (1, 2))),
        "gain": jnp.clip(1.0 + 0.18 * jax.random.normal(streams_of[7], (HD,), jnp.float32), 0.1, 1.9),
        "w_out": bell_draw(streams_of[8], (HD, D), HD ** -0.5, 0.1875, ((0, 2),)),
    }


epsilon = 1e-05

def reference(inputs, cand_user, event_user, event_count, w_qu, keys, values, gain, w_out):
    score_scale = 1.0 / math.sqrt(DH)
    proj = jax.nn.silu(jnp.dot(inputs, w_qu.reshape(D, 2 * HD), preferred_element_type=jnp.float32))
    query = proj[:, :HD].astype(jnp.bfloat16)
    gate_u = proj[:, HD:].astype(jnp.bfloat16)
    query_heads = query.astype(jnp.float32).reshape(CANDS, HEADS, DH)
    shard_keys = keys.reshape(SHARDS, EV_DEV, HEADS, DH)
    shard_values = values.reshape(SHARDS, EV_DEV, HEADS, DH)
    shard_users = event_user.reshape(SHARDS, EV_DEV)
    slot_index = jnp.arange(EV_DEV, dtype=jnp.int32)

    def accumulate(running_sum, shard_data):
        key_block, value_block, user_block, filled = shard_data
        live = (cand_user[:, None] == user_block[None, :]) & (slot_index < filled)[None, :]
        scores = jnp.einsum('chd,ehd->hce', query_heads, key_block.astype(jnp.float32)) * score_scale
        weight = (jax.nn.silu(scores) * live.astype(jnp.float32)[None]).astype(jnp.bfloat16)
        weight = lax.optimization_barrier(weight).astype(jnp.float32)
        partial_out = jnp.einsum('hce,ehd->chd', weight, value_block.astype(jnp.float32))
        return (running_sum + partial_out.reshape(CANDS, HD), None)
    initial = jnp.zeros((CANDS, HD), jnp.float32)
    attended, unused = lax.scan(accumulate, initial, (shard_keys, shard_values, shard_users, event_count))
    average = lax.optimization_barrier(jnp.sum(attended, axis=1)) / HD
    variance = lax.optimization_barrier(jnp.sum(attended * attended, axis=1)) / HD - average * average
    normed = (attended - average[:, None]) * lax.rsqrt(variance + epsilon)[:, None] * gain
    gated = (normed * gate_u.astype(jnp.float32)).astype(jnp.bfloat16)
    projected = jnp.dot(gated, w_out, preferred_element_type=jnp.float32)
    return (inputs.astype(jnp.float32) + projected).astype(jnp.bfloat16)
```

```python
import math

import jax
import jax.numpy as jnp
from jax import lax
from jax.sharding import PartitionSpec as P

DH = 128
HD = 1024


epsilon = 1e-05


def partner_sum(x):
    n = lax.axis_size("heads")
    other = lax.ppermute(x, "heads", [(i, (i + 1) % n) for i in range(n)])
    return x + other


def shards(inputs, cand_user, event_user, event_count, w_qu, keys, values, gain, w_out):
    row_count = inputs.shape[0]
    feat_width = inputs.shape[1]
    local_width = w_qu.shape[2]
    heads_here = local_width // DH
    slot_total = keys.shape[0]
    n_ev = lax.axis_size("events")
    score_scale = 1.0 / math.sqrt(DH)

    packed_weight = w_qu.reshape(feat_width, 2 * local_width)
    proj = jax.nn.silu(jnp.dot(inputs, packed_weight, preferred_element_type=jnp.float32))
    query_local = proj[:, :local_width].astype(jnp.bfloat16)
    gate_values = proj[:, local_width:].astype(jnp.bfloat16)

    spread = jnp.broadcast_to(query_local[None], (n_ev, row_count, local_width))
    queries = lax.all_to_all(spread, "events", 0, 0, tiled=False).reshape(n_ev * row_count, local_width)

    slot_index = jnp.arange(slot_total, dtype=jnp.int32)
    slot_valid = slot_index < event_count[0]
    key_heads = keys.reshape(slot_total, heads_here, DH)
    value_heads = values.reshape(slot_total, heads_here, DH)
    all_rows = queries.shape[0]
    query_block = queries.reshape(all_rows, heads_here, DH)
    user_match = ((cand_user[:, None] == event_user[None, :]) & slot_valid[None, :]).astype(jnp.float32)
    scores = (
        jnp.einsum("chd,ehd->hce", query_block, key_heads, preferred_element_type=jnp.float32)
        * score_scale
    )
    attn_weights = (jax.nn.silu(scores) * user_match[None]).astype(jnp.bfloat16)
    partial_out = jnp.einsum(
        "hce,ehd->chd", attn_weights, value_heads, preferred_element_type=jnp.float32
    ).reshape(n_ev, row_count, local_width)

    pieces = lax.all_to_all(partial_out, "events", 0, 0, tiled=False)
    attended = jnp.sum(pieces, axis=0)

    moments = jnp.stack([jnp.sum(attended, axis=1), jnp.sum(attended * attended, axis=1)])
    moments = partner_sum(moments)
    average = moments[0] / HD
    variance = moments[1] / HD - average * average
    normed = (attended - average[:, None]) * lax.rsqrt(variance + epsilon)[:, None] * gain
    gated = (normed * gate_values.astype(jnp.float32)).astype(jnp.bfloat16)
    projected = jnp.dot(gated, w_out, preferred_element_type=jnp.float32)
    summed_heads = partner_sum(projected)
    return (inputs.astype(jnp.float32) + summed_heads).astype(jnp.bfloat16)


def solution(mesh):
    placed = (
        P(("groups", "events"), None),
        P("groups"),
        P(("groups", "events")),
        P(("groups", "events")),
        P(None, None, "heads"),
        P(("groups", "events"), "heads"),
        P(("groups", "events"), "heads"),
        P("heads"),
        P("heads", None),
    )
    return jax.shard_map(
        shards, mesh=mesh, in_specs=placed, out_specs=P(("groups", "events"), None), check_vma=False
    )
```

```python
import math

import jax
import jax.numpy as jnp
from jax import lax
from jax.sharding import PartitionSpec as P

DH = 128
HD = 1024


epsilon = 1e-05


def partner_sum(x):
    n = lax.axis_size("heads")
    other = lax.ppermute(x, "heads", [(i, (i + 1) % n) for i in range(n)])
    return x + other


def shards(inputs, cand_user, event_user, event_count, w_qu, keys, values, gain, w_out):
    row_count = inputs.shape[0]
    feat_width = inputs.shape[1]
    local_width = w_qu.shape[2]
    heads_here = local_width // DH
    slot_total = keys.shape[0]
    n_ev = lax.axis_size("events")
    score_scale = 1.0 / math.sqrt(DH)

    packed_weight = w_qu.reshape(feat_width, 2 * local_width)
    proj = jax.nn.silu(jnp.dot(inputs, packed_weight, preferred_element_type=jnp.float32))
    query_local = proj[:, :local_width].astype(jnp.bfloat16)
    gate_values = proj[:, local_width:].astype(jnp.bfloat16)

    spread = jnp.broadcast_to(query_local[None], (n_ev, row_count, local_width))
    queries = lax.all_to_all(spread, "events", 0, 0, tiled=False).reshape(n_ev * row_count, local_width)

    slot_index = jnp.arange(slot_total, dtype=jnp.int32)
    slot_valid = slot_index < event_count[0]
    key_heads = keys.reshape(slot_total, heads_here, DH)
    value_heads = values.reshape(slot_total, heads_here, DH)
    all_rows = queries.shape[0]
    query_block = queries.reshape(all_rows, heads_here, DH)
    user_match = ((cand_user[:, None] == event_user[None, :]) & slot_valid[None, :]).astype(jnp.float32)
    scores = (
        jnp.einsum("chd,ehd->hce", query_block, key_heads, preferred_element_type=jnp.float32)
        * score_scale
    )
    attn_weights = (jax.nn.silu(scores) * user_match[None]).astype(jnp.bfloat16)
    partial_out = jnp.einsum(
        "hce,ehd->chd", attn_weights, value_heads, preferred_element_type=jnp.float32
    ).reshape(n_ev, row_count, local_width)

    pieces = lax.all_to_all(partial_out.astype(jnp.bfloat16), "events", 0, 0, tiled=False)
    attended = jnp.sum(pieces.astype(jnp.float32), axis=0)

    moments = jnp.stack([jnp.sum(attended, axis=1), jnp.sum(attended * attended, axis=1)])
    moments = partner_sum(moments)
    average = moments[0] / HD
    variance = moments[1] / HD - average * average
    normed = (attended - average[:, None]) * lax.rsqrt(variance + epsilon)[:, None] * gain
    gated = (normed * gate_values.astype(jnp.float32)).astype(jnp.bfloat16)
    projected = jnp.dot(gated, w_out, preferred_element_type=jnp.float32)
    summed_heads = partner_sum(projected)
    return (inputs.astype(jnp.float32) + summed_heads).astype(jnp.bfloat16)


def solution(mesh):
    placed = (
        P(("groups", "events"), None),
        P("groups"),
        P(("groups", "events")),
        P(("groups", "events")),
        P(None, None, "heads"),
        P(("groups", "events"), "heads"),
        P(("groups", "events"), "heads"),
        P("heads"),
        P("heads", None),
    )
    return jax.shard_map(
        shards, mesh=mesh, in_specs=placed, out_specs=P(("groups", "events"), None), check_vma=False
    )
```

```python
import math

import jax
import jax.numpy as jnp
from jax import lax
from jax.sharding import PartitionSpec as P

DH = 128
HD = 1024


epsilon = 1e-05


def swap(x):
    n = lax.axis_size("heads")
    return lax.ppermute(x, "heads", [(i, (i + 1) % n) for i in range(n)])


def shards(inputs, cand_user, event_user, event_count, w_qu, keys, values, gain, w_out):
    row_count = inputs.shape[0]
    feat_width = inputs.shape[1]
    local_width = w_qu.shape[2]
    heads_here = local_width // DH
    slot_total = keys.shape[0]
    n_ev = lax.axis_size("events")
    score_scale = 1.0 / math.sqrt(DH)

    packed_weight = w_qu.reshape(feat_width, 2 * local_width)
    proj = jax.nn.silu(jnp.dot(inputs, packed_weight, preferred_element_type=jnp.float32))
    query_local = proj[:, :local_width].astype(jnp.bfloat16)
    gate_values = proj[:, local_width:].astype(jnp.bfloat16)

    spread = jnp.broadcast_to(query_local[None], (n_ev, row_count, local_width))
    queries = lax.all_to_all(spread, "events", 0, 0, tiled=False).reshape(n_ev * row_count, local_width)

    slot_index = jnp.arange(slot_total, dtype=jnp.int32)
    slot_valid = slot_index < event_count[0]
    key_heads = keys.reshape(slot_total, heads_here, DH)
    value_heads = values.reshape(slot_total, heads_here, DH)
    all_rows = queries.shape[0]
    query_block = queries.reshape(all_rows, heads_here, DH)
    user_match = ((cand_user[:, None] == event_user[None, :]) & slot_valid[None, :]).astype(jnp.float32)
    scores = (
        jnp.einsum("chd,ehd->hce", query_block, key_heads, preferred_element_type=jnp.float32)
        * score_scale
    )
    attn_weights = (jax.nn.silu(scores) * user_match[None]).astype(jnp.bfloat16)
    partial_out = jnp.einsum(
        "hce,ehd->chd", attn_weights, value_heads, preferred_element_type=jnp.float32
    ).reshape(n_ev, row_count, local_width)

    pieces = lax.all_to_all(partial_out.astype(jnp.bfloat16), "events", 0, 0, tiled=False)
    attended = jnp.sum(pieces.astype(jnp.float32), axis=0)

    first = jnp.sum(attended, axis=1)
    second = jnp.sum(attended * attended, axis=1)
    weighting = gain * gate_values.astype(jnp.float32)
    centred = (attended - (first / local_width)[:, None]) * weighting
    lhs = jnp.concatenate([centred, weighting], axis=0).astype(jnp.bfloat16)
    terms = jnp.dot(lhs, w_out, preferred_element_type=jnp.float32)
    packet = jnp.concatenate([terms.reshape(-1), first, second])
    other = swap(packet)
    cut = terms.size
    terms_other = other[:cut].reshape(terms.shape)
    first_other = other[cut:cut + row_count]
    second_other = other[cut + row_count:]

    average = (first + first_other) / HD
    variance = (second + second_other) / HD - average * average
    scale = lax.rsqrt(variance + epsilon)
    centred_sum = terms[:row_count] + terms_other[:row_count]
    shift = (average - first / local_width)[:, None] * terms[row_count:] + (
        average - first_other / local_width
    )[:, None] * terms_other[row_count:]
    summed_heads = scale[:, None] * (centred_sum - shift)
    return (inputs.astype(jnp.float32) + summed_heads).astype(jnp.bfloat16)


def solution(mesh):
    placed = (
        P(("groups", "events"), None),
        P("groups"),
        P(("groups", "events")),
        P(("groups", "events")),
        P(None, None, "heads"),
        P(("groups", "events"), "heads"),
        P(("groups", "events"), "heads"),
        P("heads"),
        P("heads", None),
    )
    return jax.shard_map(
        shards, mesh=mesh, in_specs=placed, out_specs=P(("groups", "events"), None), check_vma=False
    )
```
